256 devices in a mesh: hst: 64 (over x, z, core), local: 4 (over y).
Axes of the slice: x: 4, y: 4, z: 8, core: 2. Of those that a mesh axis runs over, the one named last changes fastest.
Arguments:
- patches: bfloat16 [262144, 768], P(('hst', 'local')), may hold values from -6 to 6
- w_in: bfloat16 [768, 3072], replicated, may hold values from -0.21875 to 0.21875
- b_in: float32 [3072], replicated, may hold values from -3 to 3
- w_out: bfloat16 [3072, 512], replicated, may hold values from -0.15625 to 0.15625
- b_out: float32 [512], replicated, may hold values from -3 to 3
- ema_sums: float32 [262144, 512], P(('hst', 'local')), may hold values from -12 to 12
- ema_counts: float32 [262144], P(('hst', 'local')), may hold values from 0.5 to 4
- code_ids: int32 [262144], P(('hst', 'local')), may hold values from 0 to 262143, as said below
Outputs:
- codebook: float32 [262144, 512], P(('hst', 'local'))
- new_counts: float32 [262144], P(('hst', 'local'))
- quantized: bfloat16 [262144, 512], P(('hst', 'local'))
The draws below stay inside these ranges and needn't reach their ends.
Inputs may be any that keep to these rules, and one draw needn't show every extreme that they name: `code_ids`: in each aligned block of 1024 patches (the patches of one device), at most 8 ids lie in any one range [k * 1024, (k + 1) * 1024); one such range gets exactly 8 from every block.
All inputs are finite; a program needn't handle non-finite values.
Results may differ from the reference program's by a relative error of at most 0.002.
Values may be sent and summed in bfloat16 or wider, within the bound.
No kernel may reach another device: no remote copies, remote signals or barrier semaphores. Data moves between devices by JAX's collectives and lax.ppermute only.
A program may use at most 64 MiB of HBM per device.

```python
import math
import jax
import jax.numpy as jnp
from jax import lax

D_IN = 768
HIDDEN_SIZE = 3072
D_LAT = 512
CODES_DEV = 1024
P_DEV = 1024
OWNERS = 256
CAP = 8
PATCHES = 262144
CODES = 262144


def draw_code_ids(key, part):
    slot_total = OWNERS * CAP
    hot_owner = jax.random.randint(jax.random.fold_in(key, 1), (), 0, OWNERS)
    owner_weight = jax.random.randint(jax.random.fold_in(key, 2), (OWNERS,), 0, 1024)
    slot_owner = jnp.arange(slot_total) // CAP
    slot_number = jnp.arange(slot_total)

    def one_source(src_key):
        base_score = jax.random.randint(jax.random.fold_in(src_key, 3), (slot_total,), 0, 1024)
        score = (base_score + owner_weight[slot_owner]) * slot_total + slot_number
        score = jnp.where(slot_owner == hot_owner, -1 - slot_number, score)
        unused, picked = lax.top_k(score, P_DEV - CAP)
        row_owner = jnp.concatenate([jnp.full((CAP,), hot_owner, jnp.int32), slot_owner[picked].astype(jnp.int32)])
        row_owner = jax.random.permutation(jax.random.fold_in(src_key, 4), row_owner)
        exponent = jax.random.randint(jax.random.fold_in(src_key, 5), (P_DEV,), 0, 11)
        limit = jnp.minimum(jnp.power(2, exponent), CODES_DEV)
        offsets = jax.random.randint(jax.random.fold_in(src_key, 6), (P_DEV,), 0, limit)
        return row_owner * CODES_DEV + offsets
    source_keys = jax.random.split(jax.random.fold_in(key, 9), OWNERS)
    return jax.vmap(one_source)(source_keys).reshape(-1).astype(jnp.int32)


def steps_of(stream_key, extent, cuts, least, top_value):
    level, own = 1.0, jax.random.fold_in(stream_key, 6)
    for axis_at, blocks in cuts:
        draws = jnp.exp(jax.random.uniform(jax.random.fold_in(own, axis_at), (blocks,), jnp.float32, least / len(cuts), top_value / len(cuts)))
        level = level * jnp.repeat(draws, extent[axis_at] // blocks).reshape([-1 if axis == axis_at else 1 for axis in range(len(extent))])
    return level


def gaussian(key, dims, deviation, most, cuts=(), held_as=jnp.bfloat16):
    entries = deviation * jax.random.normal(key, dims, jnp.float32)
    if cuts:
        entries = entries * steps_of(key, dims, cuts, -0.22, 0.18)
    return jnp.clip(entries, -most, most).astype(held_as)


def setup_inputs(seed: int = 0) -> dict:
    arg_keys = jax.random.split(jax.random.key(seed), 9)
    patches = gaussian(arg_keys[0], (PATCHES, D_IN), 1.0, 6.0, ((0, 256),))
    w_in = gaussian(arg_keys[1], (D_IN, HIDDEN_SIZE), D_IN ** -0.5, 0.21875)
    b_in = gaussian(arg_keys[2], (HIDDEN_SIZE,), 0.5, 3.0, (), jnp.float32)
    w_out = gaussian(arg_keys[3], (HIDDEN_SIZE, D_LAT), (HIDDEN_SIZE // 2) ** -0.5, 0.15625)
    b_out = gaussian(arg_keys[4], (D_LAT,), 0.5, 3.0, (), jnp.float32)
    ema_sums = gaussian(arg_keys[5], (CODES, D_LAT), 2.0, 12.0, ((0, 256),), jnp.float32)
    ema_counts = jnp.clip(jnp.exp(math.log(4.0) - 2.0794415 * jax.random.uniform(arg_keys[6], (CODES,), jnp.float32) ** steps_of(arg_keys[6], (CODES,), ((0, 256),), -0.2, 0.2)), 0.5, 4.0)
    code_ids = draw_code_ids(jax.random.fold_in(arg_keys[8], 71), 0)
    return dict(patches=patches, w_in=w_in, b_in=b_in, w_out=w_out, b_out=b_out, ema_sums=ema_sums, ema_counts=ema_counts, code_ids=code_ids)


DECAY = 0.9


def reference(patches, w_in, b_in, w_out, b_out, ema_sums, ema_counts, code_ids):
    grouped = patches.reshape(OWNERS, P_DEV, D_IN)

    def encode(row_block):
        pre_act = jnp.dot(row_block, w_in, preferred_element_type=jnp.float32) + b_in
        hidden = jnp.tanh(pre_act).astype(jnp.bfloat16)
        latent = jnp.dot(hidden, w_out, preferred_element_type=jnp.float32) + b_out
        return latent.astype(jnp.bfloat16)

    latents = lax.map(encode, grouped).reshape(PATCHES, D_LAT)
    code_sums = jax.ops.segment_sum(latents.astype(jnp.float32), code_ids, num_segments=CODES)
    code_counts = jax.ops.segment_sum(jnp.ones((PATCHES,), jnp.float32), code_ids, num_segments=CODES)
    new_counts = DECAY * ema_counts + (1.0 - DECAY) * code_counts
    codebook = (DECAY * ema_sums + (1.0 - DECAY) * code_sums) / new_counts[:, None]
    quantized = codebook.astype(jnp.bfloat16)[code_ids]
    return codebook, new_counts, quantized
```

```python
import jax
import jax.numpy as jnp
from jax import lax
from jax.sharding import PartitionSpec as P

DECAY = 0.9
AXES = ("hst", "local")
EXTRA = 128


def per_device(patches, w_in, b_in, w_out, b_out, ema_sums, ema_counts, code_ids):
    owner_count = lax.axis_size(AXES)
    code_span = ema_sums.shape[0]
    latent_width = ema_sums.shape[1]
    row_count = patches.shape[0]
    capacity = max(2, 2 * row_count // owner_count)
    slot_count = owner_count * capacity

    pre_act = jnp.dot(patches, w_in, preferred_element_type=jnp.float32) + b_in
    hidden = jnp.tanh(pre_act).astype(jnp.bfloat16)
    latents = (jnp.dot(hidden, w_out, preferred_element_type=jnp.float32) + b_out).astype(
        jnp.bfloat16
    )

    owner_of = code_ids // code_span
    offset = code_ids - owner_of * code_span
    rows = jnp.arange(row_count)
    same = (owner_of[:, None] == owner_of[None, :]) & (rows[None, :] < rows[:, None])
    position = jnp.sum(same.astype(jnp.int32), axis=1)
    slot_index = owner_of * capacity + position
    placing_t = (slot_index[:, None] == jnp.arange(slot_count)[None, :]).astype(jnp.bfloat16)

    lane = jnp.arange(EXTRA)[None, :]
    hi = (offset // 32 + 1).astype(jnp.float32)[:, None]
    lo = (offset % 32).astype(jnp.float32)[:, None]
    extra = jnp.where(lane == 0, 1.0, jnp.where(lane == 1, hi, jnp.where(lane == 2, lo, 0.0)))
    payload = jnp.concatenate([latents, extra.astype(jnp.bfloat16)], axis=1)
    outgoing = lax.dot_general(
        placing_t, payload, (((0,), (0,)), ((), ())), preferred_element_type=jnp.float32
    ).astype(jnp.bfloat16)
    outgoing = outgoing.reshape(owner_count, capacity, latent_width + EXTRA)
    arrived = lax.all_to_all(outgoing, AXES, 0, 0, tiled=True)
    arrived = arrived.reshape(slot_count, latent_width + EXTRA)

    got_hi = arrived[:, latent_width + 1].astype(jnp.int32)
    got_lo = arrived[:, latent_width + 2].astype(jnp.int32)
    got_offset = (got_hi - 1) * 32 + got_lo
    chosen = (got_offset[:, None] == jnp.arange(code_span)[None, :]).astype(jnp.bfloat16)
    totals = lax.dot_general(
        chosen, arrived, (((0,), (0,)), ((), ())), preferred_element_type=jnp.float32
    )
    code_sums = totals[:, :latent_width]
    code_counts = totals[:, latent_width]
    new_counts = DECAY * ema_counts + (1.0 - DECAY) * code_counts
    codebook = (DECAY * ema_sums + (1.0 - DECAY) * code_sums) / new_counts[:, None]
    replies = jnp.dot(
        chosen, codebook.astype(jnp.bfloat16), preferred_element_type=jnp.float32
    ).astype(jnp.bfloat16)
    replies = replies.reshape(owner_count, capacity, latent_width)
    returned = lax.all_to_all(replies, AXES, 0, 0, tiled=True)
    returned = returned.reshape(slot_count, latent_width)
    quantized = jnp.dot(placing_t, returned, preferred_element_type=jnp.float32).astype(
        jnp.bfloat16
    )
    return (codebook, new_counts, quantized)


def solution(mesh):
    in_specs = (
        P(AXES, None),
        P(),
        P(),
        P(),
        P(),
        P(AXES, None),
        P(AXES),
        P(AXES),
    )
    out_specs = (P(AXES, None), P(AXES), P(AXES, None))
    return jax.shard_map(
        per_device, mesh=mesh, in_specs=in_specs, out_specs=out_specs, check_vma=False
    )
```

```python
import jax
import jax.numpy as jnp
from jax import lax
from jax.sharding import PartitionSpec as P

DECAY = 0.9
AXES = ("hst", "local")
EXTRA = 128


def per_device(patches, w_in, b_in, w_out, b_out, ema_sums, ema_counts, code_ids):
    owner_count = lax.axis_size(AXES)
    code_span = ema_sums.shape[0]
    latent_width = ema_sums.shape[1]
    row_count = patches.shape[0]
    capacity = max(2, 2 * row_count // owner_count)
    slot_count = owner_count * capacity

    pre_act = jnp.dot(patches, w_in, preferred_element_type=jnp.float32) + b_in
    hidden = jnp.tanh(pre_act).astype(jnp.bfloat16)
    latents = (jnp.dot(hidden, w_out, preferred_element_type=jnp.float32) + b_out).astype(
        jnp.bfloat16
    )

    owner_of = code_ids // code_span
    offset = code_ids - owner_of * code_span
    rows = jnp.arange(row_count)
    same = (owner_of[:, None] == owner_of[None, :]) & (rows[None, :] < rows[:, None])
    position = jnp.sum(same.astype(jnp.int32), axis=1)
    slot_index = owner_of * capacity + position
    placing_t = (slot_index[:, None] == jnp.arange(slot_count)[None, :]).astype(jnp.bfloat16)

    lane = jnp.arange(EXTRA)[None, :]
    hi = (offset // 32 + 1).astype(jnp.float32)[:, None]
    lo = (offset % 32).astype(jnp.float32)[:, None]
    extra = jnp.where(lane == 0, 1.0, jnp.where(lane == 1, hi, jnp.where(lane == 2, lo, 0.0)))
    payload = jnp.concatenate([latents, extra.astype(jnp.bfloat16)], axis=1)
    outgoing = lax.dot_general(
        placing_t, payload, (((0,), (0,)), ((), ())), preferred_element_type=jnp.float32
    ).astype(jnp.bfloat16)
    outgoing = outgoing.reshape(owner_count, capacity, latent_width + EXTRA)
    arrived = lax.all_to_all(outgoing, AXES, 0, 0, tiled=True)
    arrived = arrived.reshape(slot_count, latent_width + EXTRA)

    weight = jnp.where(lane == 1, 32.0, jnp.where(lane == 2, 1.0, 0.0))
    got_offset = jnp.sum(arrived[:, latent_width:].astype(jnp.float32) * weight, axis=1)
    got_offset = got_offset.astype(jnp.int32) - 32
    chosen = (got_offset[:, None] == jnp.arange(code_span)[None, :]).astype(jnp.bfloat16)
    totals = lax.dot_general(
        chosen, arrived, (((0,), (0,)), ((), ())), preferred_element_type=jnp.float32
    )
    code_sums = totals[:, :latent_width]
    code_counts = totals[:, latent_width]
    new_counts = DECAY * ema_counts + (1.0 - DECAY) * code_counts
    codebook = (DECAY * ema_sums + (1.0 - DECAY) * code_sums) / new_counts[:, None]
    replies = jnp.dot(
        chosen, codebook.astype(jnp.bfloat16), preferred_element_type=jnp.float32
    ).astype(jnp.bfloat16)
    replies = replies.reshape(owner_count, capacity, latent_width)
    returned = lax.all_to_all(replies, AXES, 0, 0, tiled=True)
    returned = returned.reshape(slot_count, latent_width)
    quantized = jnp.dot(placing_t, returned, preferred_element_type=jnp.float32).astype(
        jnp.bfloat16
    )
    return (codebook, new_counts, quantized)


def solution(mesh):
    in_specs = (
        P(AXES, None),
        P(),
        P(),
        P(),
        P(),
        P(AXES, None),
        P(AXES),
        P(AXES),
    )
    out_specs = (P(AXES, None), P(AXES), P(AXES, None))
    return jax.shard_map(
        per_device, mesh=mesh, in_specs=in_specs, out_specs=out_specs, check_vma=False
    )
```

```python
import jax
import jax.numpy as jnp
from jax import lax
from jax.sharding import PartitionSpec as P

DECAY = 0.9
AXES = ("hst", "local")
EXTRA = 128


def per_device(patches, w_in, b_in, w_out, b_out, ema_sums, ema_counts, code_ids):
    owner_count = lax.axis_size(AXES)
    code_span = ema_sums.shape[0]
    latent_width = ema_sums.shape[1]
    row_count = patches.shape[0]
    capacity = max(2, 2 * row_count // owner_count)
    slot_count = owner_count * capacity

    pre_act = jnp.dot(patches, w_in, preferred_element_type=jnp.float32) + b_in
    hidden = jnp.tanh(pre_act).astype(jnp.bfloat16)
    latents = (jnp.dot(hidden, w_out, preferred_element_type=jnp.float32) + b_out).astype(
        jnp.bfloat16
    )

    owner_of = code_ids // code_span
    offset = code_ids - owner_of * code_span
    rows = jnp.arange(row_count)
    same = (owner_of[:, None] == owner_of[None, :]) & (rows[None, :] < rows[:, None])
    position = jnp.sum(same.astype(jnp.int32), axis=1)
    local_count = lax.axis_size("local")
    host_count = owner_count // local_count
    chunk = (owner_of % local_count) * host_count + owner_of // local_count
    slot_index = chunk * capacity + position
    placing_t = (slot_index[:, None] == jnp.arange(slot_count)[None, :]).astype(jnp.bfloat16)

    lane = jnp.arange(EXTRA)[None, :]
    hi = (offset // 32 + 1).astype(jnp.float32)[:, None]
    lo = (offset % 32).astype(jnp.float32)[:, None]
    extra = jnp.where(lane == 0, 1.0, jnp.where(lane == 1, hi, jnp.where(lane == 2, lo, 0.0)))
    payload = jnp.concatenate([latents, extra.astype(jnp.bfloat16)], axis=1)
    outgoing = lax.dot_general(
        placing_t, payload, (((0,), (0,)), ((), ())), preferred_element_type=jnp.float32
    ).astype(jnp.bfloat16)
    outgoing = outgoing.reshape(owner_count, capacity, latent_width + EXTRA)
    arrived = lax.all_to_all(outgoing, ("local", "hst"), 0, 0, tiled=True)
    arrived = arrived.reshape(slot_count, latent_width + EXTRA)

    weight = jnp.where(lane == 1, 32.0, jnp.where(lane == 2, 1.0, 0.0))
    got_offset = jnp.sum(arrived[:, latent_width:].astype(jnp.float32) * weight, axis=1)
    got_offset = got_offset.astype(jnp.int32) - 32
    chosen = (got_offset[:, None] == jnp.arange(code_span)[None, :]).astype(jnp.bfloat16)
    totals = lax.dot_general(
        chosen, arrived, (((0,), (0,)), ((), ())), preferred_element_type=jnp.float32
    )
    code_sums = totals[:, :latent_width]
    code_counts = totals[:, latent_width]
    new_counts = DECAY * ema_counts + (1.0 - DECAY) * code_counts
    codebook = (DECAY * ema_sums + (1.0 - DECAY) * code_sums) / new_counts[:, None]
    replies = jnp.dot(
        chosen, codebook.astype(jnp.bfloat16), preferred_element_type=jnp.float32
    ).astype(jnp.bfloat16)
    replies = replies.reshape(owner_count, capacity, latent_width)
    returned = lax.all_to_all(replies, ("local", "hst"), 0, 0, tiled=True)
    returned = returned.reshape(slot_count, latent_width)
    quantized = jnp.dot(placing_t, returned, preferred_element_type=jnp.float32).astype(
        jnp.bfloat16
    )
    return (codebook, new_counts, quantized)


def solution(mesh):
    in_specs = (
        P(AXES, None),
        P(),
        P(),
        P(),
        P(),
        P(AXES, None),
        P(AXES),
        P(AXES),
    )
    out_specs = (P(AXES, None), P(AXES), P(AXES, None))
    return jax.shard_map(
        per_device, mesh=mesh, in_specs=in_specs, out_specs=out_specs, check_vma=False
    )
```

```python
import jax
import jax.numpy as jnp
from jax import lax
from jax.sharding import PartitionSpec as P

DECAY = 0.9
AXES = ("hst", "local")
EXTRA = 128


def per_device(patches, w_in, b_in, w_out, b_out, ema_sums, ema_counts, code_ids):
    owner_count = lax.axis_size(AXES)
    code_span = ema_sums.shape[0]
    latent_width = ema_sums.shape[1]
    row_count = patches.shape[0]
    capacity = max(2, 2 * row_count // owner_count)
    slot_count = owner_count * capacity

    pre_act = jnp.dot(patches, w_in, preferred_element_type=jnp.float32) + b_in
    hidden = jnp.tanh(pre_act).astype(jnp.bfloat16)
    latents = (jnp.dot(hidden, w_out, preferred_element_type=jnp.float32) + b_out).astype(
        jnp.bfloat16
    )

    owner_of = code_ids // code_span
    offset = code_ids - owner_of * code_span
    rows = jnp.arange(row_count)
    same = (owner_of[:, None] == owner_of[None, :]) & (rows[None, :] < rows[:, None])
    position = jnp.sum(same.astype(jnp.int32), axis=1)
    local_count = lax.axis_size("local")
    host_count = owner_count // local_count
    chunk = (owner_of % local_count) * host_count + owner_of // local_count
    slot_index = chunk * capacity + position
    placing_t = (slot_index[:, None] == jnp.arange(slot_count)[None, :]).astype(jnp.bfloat16)

    lane = jnp.arange(EXTRA)[None, :]
    hi = (offset // 32 + 1).astype(jnp.float32)[:, None]
    lo = (offset % 32).astype(jnp.float32)[:, None]
    extra = jnp.where(lane == 0, 1.0, jnp.where(lane == 1, hi, jnp.where(lane == 2, lo, 0.0)))
    payload = jnp.concatenate([latents, extra.astype(jnp.bfloat16)], axis=1)
    outgoing = lax.dot_general(
        placing_t, payload, (((0,), (0,)), ((), ())), preferred_element_type=jnp.float32
    ).astype(jnp.bfloat16)
    outgoing = outgoing.reshape(owner_count, capacity, latent_width + EXTRA)
    arrived = lax.all_to_all(outgoing, ("local", "hst"), 0, 0, tiled=True)
    arrived = arrived.reshape(slot_count, latent_width + EXTRA)

    weight = jnp.where(lane == 1, 32.0, jnp.where(lane == 2, 1.0, 0.0))
    got_offset = jnp.sum(arrived[:, latent_width:].astype(jnp.float32) * weight, axis=1)
    got_offset = got_offset.astype(jnp.int32) - 32
    chosen = (got_offset[:, None] == jnp.arange(code_span)[None, :]).astype(jnp.bfloat16)
    totals = lax.dot_general(
        chosen, arrived, (((0,), (0,)), ((), ())), preferred_element_type=jnp.float32
    )
    code_sums = totals[:, :latent_width]
    code_counts = totals[:, latent_width]
    new_counts = DECAY * ema_counts + (1.0 - DECAY) * code_counts
    for_replies = (DECAY * ema_sums + (1.0 - DECAY) * code_sums) / new_counts[:, None]
    replies = jnp.dot(
        chosen, for_replies.astype(jnp.bfloat16), preferred_element_type=jnp.float32
    ).astype(jnp.bfloat16)
    again, again_offset, again_counts = lax.optimization_barrier((arrived, got_offset, new_counts))
    again_chosen = (again_offset[:, None] == jnp.arange(code_span)[None, :]).astype(jnp.bfloat16)
    again_totals = lax.dot_general(
        again_chosen, again, (((0,), (0,)), ((), ())), preferred_element_type=jnp.float32
    )
    codebook = (
        DECAY * ema_sums + (1.0 - DECAY) * again_totals[:, :latent_width]
    ) / again_counts[:, None]
    replies = replies.reshape(owner_count, capacity, latent_width)
    returned = lax.all_to_all(replies, ("local", "hst"), 0, 0, tiled=True)
    returned = returned.reshape(slot_count, latent_width)
    quantized = jnp.dot(placing_t, returned, preferred_element_type=jnp.float32).astype(
        jnp.bfloat16
    )
    return (codebook, new_counts, quantized)


def solution(mesh):
    in_specs = (
        P(AXES, None),
        P(),
        P(),
        P(),
        P(),
        P(AXES, None),
        P(AXES),
        P(AXES),
    )
    out_specs = (P(AXES, None), P(AXES), P(AXES, None))
    return jax.shard_map(
        per_device, mesh=mesh, in_specs=in_specs, out_specs=out_specs, check_vma=False
    )
```
